32 devices in a mesh: col: 8 (over y, x, core), row: 4 (over z).
Axes of the slice: x: 2, y: 2, z: 4, core: 2. Of those that a mesh axis runs over, the one named last changes fastest.
Arguments:
- p_blocks: bfloat16 [4, 72, 4096], P('row', 'col'), may hold values from -0.5390625 to 0.5390625
- p_slots: int32 [4, 72], P('row', 'col'), may hold values from 0 to 18, as said below
- out_slots: int32 [4, 104], P('row', 'col'), may hold values from 0 to 18, as said below
Outputs:
- purified: float32 [4, 104, 4096], P('row', 'col')
The draws below stay inside these ranges and needn't reach their ends.
Inputs may be any that keep to these rules, and one draw needn't show every extreme that they name: `p_slots`: on each device the used slots (entries below 18) come first and name distinct positions; the remaining slots hold 18. Each device uses between half of its 9 slots (rounded up) and all of them, and some device uses all. `out_slots`: on each device the used slots (entries below 18) come first and name distinct positions; the remaining slots hold 18. Each device uses between half of its 13 slots (rounded up) and all of them, and some device uses all.
All inputs are finite; a program needn't handle non-finite values.
Results may differ from the reference program's by a relative error of at most 0.0003.
Values may be sent and summed in bfloat16 or wider, within the bound.
No kernel may reach another device: no remote copies, remote signals or barrier semaphores. Data moves between devices by JAX's collectives and lax.ppermute only.
A program may use at most 192 MiB of HBM per device.

```python
import jax
import jax.numpy as jnp
from jax import lax

BLK = 64
COLS_DEV = 3
NB = 24
ROWS_DEV = 6
CAP = 9
OUT_CAP = 13
N_COL = 8
N_ROW = 4


def slot_table(key, cells, capacity):
    devices_all = N_ROW * N_COL
    key_list = jax.random.split(key, devices_all + 2)
    shuffled = jax.vmap(lambda single: jax.random.permutation(single, cells))(key_list[:devices_all])
    shuffled = shuffled[:, :capacity].astype(jnp.int32)
    used_count = jax.random.randint(key_list[devices_all], (devices_all,), (capacity + 1) // 2, capacity + 1)
    busiest = jax.random.randint(key_list[devices_all + 1], (), 0, devices_all)
    used_count = jnp.where(jnp.arange(devices_all) == busiest, capacity, used_count)
    table = jnp.where(jnp.arange(capacity)[None, :] < used_count[:, None], shuffled, cells)
    return table.reshape(N_ROW, N_COL * capacity).astype(jnp.int32)


def draw_p_slots(key, part):
    return slot_table(jax.random.fold_in(key, 11), ROWS_DEV * COLS_DEV, CAP)


def draw_out_slots(key, part):
    return slot_table(jax.random.fold_in(key, 23), ROWS_DEV * COLS_DEV, OUT_CAP)


def block_levels(rng, dims, pieces, low, largest):
    level, own = 1.0, jax.random.fold_in(rng, 6)
    for dim, blocks in pieces:
        draws = jnp.exp(jax.random.uniform(jax.random.fold_in(own, dim), (blocks,), jnp.float32, low / len(pieces), largest / len(pieces)))
        level = level * jnp.repeat(draws, dims[dim] // blocks).reshape([-1 if axis == dim else 1 for axis in range(len(dims))])
    return level


def noise(key, shape, scale, reach, cuts=(), held_as=jnp.bfloat16):
    factor_of = block_levels(key, shape, cuts, -0.22, 0.18) if cuts else 1.0
    values = jax.random.normal(key, shape, jnp.float32) * scale * factor_of
    return jnp.minimum(jnp.maximum(values, -reach), reach).astype(held_as)


def setup_inputs(seed: int = 0) -> dict:
    splits = jax.random.split(jax.random.key(seed), 4)
    return {
        "p_blocks": noise(splits[0], (N_ROW, N_COL * CAP, BLK * BLK), 0.09, 0.5390625, ((0, 4), (1, 8))),
        "p_slots": draw_p_slots(jax.random.fold_in(splits[3], 71), 0),
        "out_slots": draw_out_slots(jax.random.fold_in(splits[3], 71), 0),
    }


def slot_index(slot_ids, used_count):
    cells = ROWS_DEV * COLS_DEV
    table = slot_ids.reshape(N_ROW, N_COL, used_count)
    row_owner = jnp.arange(N_ROW, dtype=jnp.int32)[:, None, None]
    col_owner = jnp.arange(N_COL, dtype=jnp.int32)[None, :, None]
    block_row = row_owner * ROWS_DEV + table // COLS_DEV
    block_col = col_owner * COLS_DEV + table % COLS_DEV
    in_use = table < cells
    flat_index = jnp.where(in_use, block_row * NB + block_col, NB * NB).astype(jnp.int32)
    return flat_index.reshape(-1), in_use.reshape(-1)


def reference(p_blocks, p_slots, out_slots):
    flat_index, in_use = slot_index(p_slots, CAP)
    values = p_blocks.reshape(N_ROW * N_COL * CAP, BLK * BLK)
    grid = jnp.zeros((NB * NB, BLK * BLK), p_blocks.dtype).at[flat_index].set(values, mode="drop")
    matrix = grid.reshape(NB, NB, BLK, BLK).transpose(0, 2, 1, 3).reshape(NB * BLK, NB * BLK)
    matrix = matrix.astype(jnp.float32)
    square = jnp.dot(matrix, matrix, precision=lax.Precision.HIGHEST, preferred_element_type=jnp.float32)
    cube = jnp.dot(square, matrix, precision=lax.Precision.HIGHEST, preferred_element_type=jnp.float32)
    combined = 3.0 * square - 2.0 * cube
    new_grid = combined.reshape(NB, BLK, NB, BLK).transpose(0, 2, 1, 3).reshape(NB * NB, BLK * BLK)
    out_index, out_use = slot_index(out_slots, OUT_CAP)
    picked = new_grid[jnp.minimum(out_index, NB * NB - 1)]
    picked = jnp.where(out_use[:, None], picked, jnp.zeros_like(picked))
    return picked.reshape(N_ROW, N_COL * OUT_CAP, BLK * BLK)
```

```python
import jax
import jax.numpy as jnp
from jax import lax
from jax.sharding import PartitionSpec as P

BLK = 64
COLS_DEV = 3


def on_device(p_blocks, p_slots, out_slots):
    n_row = lax.axis_size("row")
    n_col = lax.axis_size("col")
    capacity = p_slots.shape[1]
    block_edge = BLK
    area = block_edge * block_edge
    rows_dev = COLS_DEV * n_col // n_row
    cells = rows_dev * COLS_DEV
    blocks_total = rows_dev * n_row
    width = COLS_DEV * block_edge
    height = rows_dev * block_edge

    own_ids = p_slots[0]
    id_row = jnp.zeros((1, area), jnp.bfloat16)
    id_row = id_row.at[0, :capacity].set(own_ids.astype(jnp.bfloat16))
    payload = jnp.concatenate([p_blocks[0], id_row], axis=0)

    down = lax.all_gather(payload, "row", axis=0, tiled=False)
    down_ids = down[:, capacity, :capacity].astype(jnp.int32)
    down_row = jnp.arange(n_row, dtype=jnp.int32)[:, None] * rows_dev + down_ids // COLS_DEV
    down_index = jnp.where(
        down_ids < cells, down_row * COLS_DEV + down_ids % COLS_DEV, blocks_total * COLS_DEV
    )
    column_grid = jnp.zeros((blocks_total * COLS_DEV, area), jnp.bfloat16)
    column_grid = column_grid.at[down_index.reshape(-1)].set(
        down[:, :capacity].reshape(n_row * capacity, area), mode="drop"
    )
    column_panel = (
        column_grid.reshape(blocks_total, COLS_DEV, block_edge, block_edge)
        .transpose(0, 2, 1, 3)
        .reshape(blocks_total * block_edge, width)
    )

    across = lax.all_gather(payload, "col", axis=0, tiled=False)
    across_ids = across[:, capacity, :capacity].astype(jnp.int32)
    across_col = jnp.arange(n_col, dtype=jnp.int32)[:, None] * COLS_DEV + across_ids % COLS_DEV
    across_index = jnp.where(
        across_ids < cells,
        (across_ids // COLS_DEV) * blocks_total + across_col,
        rows_dev * blocks_total,
    )
    row_grid = jnp.zeros((rows_dev * blocks_total, area), jnp.bfloat16)
    row_grid = row_grid.at[across_index.reshape(-1)].set(
        across[:, :capacity].reshape(n_col * capacity, area), mode="drop"
    )
    row_panel = (
        row_grid.reshape(rows_dev, blocks_total, block_edge, block_edge)
        .transpose(0, 2, 1, 3)
        .reshape(height, blocks_total * block_edge)
    )

    square = jnp.dot(row_panel, column_panel, preferred_element_type=jnp.float32)
    square_panel = lax.all_gather(square, "row", axis=0, tiled=True)
    cube = jnp.dot(
        row_panel.astype(jnp.float32),
        square_panel,
        precision=lax.Precision.HIGHEST,
        preferred_element_type=jnp.float32,
    )
    combined = 3.0 * square - 2.0 * cube
    new_grid = combined.reshape(rows_dev, block_edge, COLS_DEV, block_edge).transpose(0, 2, 1, 3)
    new_grid = new_grid.reshape(cells, area)
    out_ids = out_slots[0]
    picked = new_grid[jnp.minimum(out_ids, cells - 1)]
    picked = jnp.where((out_ids < cells)[:, None], picked, jnp.zeros_like(picked))
    return picked[None]


def solution(mesh):
    in_specs = (P("row", "col", None), P("row", "col"), P("row", "col"))
    out_specs = P("row", "col", None)
    return jax.shard_map(
        on_device, mesh=mesh, in_specs=in_specs, out_specs=out_specs, check_vma=False
    )
```

```python
import jax
import jax.numpy as jnp
from jax import lax
from jax.sharding import PartitionSpec as P

BLK = 64
COLS_DEV = 3


def shifted_copies(value, axis, size):
    pieces = [value]
    for shift in range(1, size):
        pairs = [(i, (i + shift) % size) for i in range(size)]
        pieces.append(lax.ppermute(value, axis, pairs))
    return jax.tree.map(lambda *xs: jnp.stack(xs), *pieces)


def on_device(p_blocks, p_slots, out_slots):
    n_row = lax.axis_size("row")
    n_col = lax.axis_size("col")
    capacity = p_slots.shape[1]
    block_edge = BLK
    area = block_edge * block_edge
    rows_dev = COLS_DEV * n_col // n_row
    cells = rows_dev * COLS_DEV
    blocks_total = rows_dev * n_row
    width = COLS_DEV * block_edge
    height = rows_dev * block_edge
    row_idx = lax.axis_index("row")
    col_idx = lax.axis_index("col")
    own = (p_blocks[0], p_slots[0])

    def shift_order(block):
        owner = block // rows_dev
        return ((row_idx - owner) % n_row) * rows_dev + block % rows_dev

    down_blocks, down_ids = shifted_copies(own, "row", n_row)
    down_row = jnp.arange(n_row, dtype=jnp.int32)[:, None] * rows_dev + down_ids // COLS_DEV
    down_index = jnp.where(
        down_ids < cells, down_row * COLS_DEV + down_ids % COLS_DEV, blocks_total * COLS_DEV
    )
    column_grid = jnp.zeros((blocks_total * COLS_DEV, area), jnp.bfloat16)
    column_grid = column_grid.at[down_index.reshape(-1)].set(
        down_blocks.reshape(n_row * capacity, area), mode="drop"
    )
    column_panel = (
        column_grid.reshape(blocks_total, COLS_DEV, block_edge, block_edge)
        .transpose(0, 2, 1, 3)
        .reshape(blocks_total * block_edge, width)
    )

    across_blocks, across_ids = shifted_copies(own, "col", n_col)
    across_src = (col_idx - jnp.arange(n_col, dtype=jnp.int32)[:, None]) % n_col
    across_col = shift_order(across_src * COLS_DEV + across_ids % COLS_DEV)
    across_index = jnp.where(
        across_ids < cells,
        (across_ids // COLS_DEV) * blocks_total + across_col,
        rows_dev * blocks_total,
    )
    row_grid = jnp.zeros((rows_dev * blocks_total, area), jnp.bfloat16)
    row_grid = row_grid.at[across_index.reshape(-1)].set(
        across_blocks.reshape(n_col * capacity, area), mode="drop"
    )
    row_panel = (
        row_grid.reshape(rows_dev, blocks_total, block_edge, block_edge)
        .transpose(0, 2, 1, 3)
        .reshape(height, blocks_total * block_edge)
    )

    square = jnp.dot(row_panel, column_panel, preferred_element_type=jnp.float32)
    square_panel = shifted_copies(square, "row", n_row).reshape(blocks_total * block_edge, width)
    cube = jnp.dot(
        row_panel.astype(jnp.float32),
        square_panel,
        precision=lax.Precision.HIGHEST,
        preferred_element_type=jnp.float32,
    )
    combined = 3.0 * square - 2.0 * cube
    new_grid = combined.reshape(rows_dev, block_edge, COLS_DEV, block_edge).transpose(0, 2, 1, 3)
    new_grid = new_grid.reshape(cells, area)
    out_ids = out_slots[0]
    picked = new_grid[jnp.minimum(out_ids, cells - 1)]
    picked = jnp.where((out_ids < cells)[:, None], picked, jnp.zeros_like(picked))
    return picked[None]


def solution(mesh):
    in_specs = (P("row", "col", None), P("row", "col"), P("row", "col"))
    out_specs = P("row", "col", None)
    return jax.shard_map(
        on_device, mesh=mesh, in_specs=in_specs, out_specs=out_specs, check_vma=False
    )
```

```python
import jax
import jax.numpy as jnp
from jax import lax
from jax.sharding import PartitionSpec as P

BLK = 64
COLS_DEV = 3


def shifted_copies(value, axis, size):
    pieces = [value]
    for shift in range(1, size):
        pairs = [(i, (i + shift) % size) for i in range(size)]
        pieces.append(lax.ppermute(value, axis, pairs))
    return jax.tree.map(lambda *xs: jnp.stack(xs), *pieces)


def on_device(p_blocks, p_slots, out_slots):
    n_row = lax.axis_size("row")
    n_col = lax.axis_size("col")
    capacity = p_slots.shape[1]
    block_edge = BLK
    area = block_edge * block_edge
    rows_dev = COLS_DEV * n_col // n_row
    cells = rows_dev * COLS_DEV
    blocks_total = rows_dev * n_row
    width = COLS_DEV * block_edge
    height = rows_dev * block_edge
    row_idx = lax.axis_index("row")
    col_idx = lax.axis_index("col")
    id_row = jnp.zeros((1, area), jnp.bfloat16)
    id_row = id_row.at[0, :capacity].set(p_slots[0].astype(jnp.bfloat16))
    own = jnp.concatenate([p_blocks[0], id_row], axis=0)

    def unpack(payloads):
        ids = payloads[:, capacity, :capacity].astype(jnp.int32)
        return payloads[:, :capacity], ids

    def shift_order(block):
        owner = block // rows_dev
        return ((row_idx - owner) % n_row) * rows_dev + block % rows_dev

    down_blocks, down_ids = unpack(shifted_copies(own, "row", n_row))
    down_row = jnp.arange(n_row, dtype=jnp.int32)[:, None] * rows_dev + down_ids // COLS_DEV
    down_index = jnp.where(
        down_ids < cells, down_row * COLS_DEV + down_ids % COLS_DEV, blocks_total * COLS_DEV
    )
    column_grid = jnp.zeros((blocks_total * COLS_DEV, area), jnp.bfloat16)
    column_grid = column_grid.at[down_index.reshape(-1)].set(
        down_blocks.reshape(n_row * capacity, area), mode="drop"
    )
    column_panel = (
        column_grid.reshape(blocks_total, COLS_DEV, block_edge, block_edge)
        .transpose(0, 2, 1, 3)
        .reshape(blocks_total * block_edge, width)
    )

    across_blocks, across_ids = unpack(shifted_copies(own, "col", n_col))
    across_src = (col_idx - jnp.arange(n_col, dtype=jnp.int32)[:, None]) % n_col
    across_col = shift_order(across_src * COLS_DEV + across_ids % COLS_DEV)
    across_index = jnp.where(
        across_ids < cells,
        (across_ids // COLS_DEV) * blocks_total + across_col,
        rows_dev * blocks_total,
    )
    row_grid = jnp.zeros((rows_dev * blocks_total, area), jnp.bfloat16)
    row_grid = row_grid.at[across_index.reshape(-1)].set(
        across_blocks.reshape(n_col * capacity, area), mode="drop"
    )
    row_panel = (
        row_grid.reshape(rows_dev, blocks_total, block_edge, block_edge)
        .transpose(0, 2, 1, 3)
        .reshape(height, blocks_total * block_edge)
    )

    square = jnp.dot(row_panel, column_panel, preferred_element_type=jnp.float32)
    square_panel = shifted_copies(square, "row", n_row).reshape(blocks_total * block_edge, width)
    cube = jnp.dot(
        row_panel.astype(jnp.float32),
        square_panel,
        precision=lax.Precision.HIGHEST,
        preferred_element_type=jnp.float32,
    )
    combined = 3.0 * square - 2.0 * cube
    new_grid = combined.reshape(rows_dev, block_edge, COLS_DEV, block_edge).transpose(0, 2, 1, 3)
    new_grid = new_grid.reshape(cells, area)
    out_ids = out_slots[0]
    picked = new_grid[jnp.minimum(out_ids, cells - 1)]
    picked = jnp.where((out_ids < cells)[:, None], picked, jnp.zeros_like(picked))
    return picked[None]


def solution(mesh):
    in_specs = (P("row", "col", None), P("row", "col"), P("row", "col"))
    out_specs = P("row", "col", None)
    return jax.shard_map(
        on_device, mesh=mesh, in_specs=in_specs, out_specs=out_specs, check_vma=False
    )
```

```python
import jax
import jax.numpy as jnp
from jax import lax
from jax.sharding import PartitionSpec as P

BLK = 64
COLS_DEV = 3


def shifted_copies(value, axis, size):
    pieces = [value]
    for shift in range(1, size):
        pairs = [(i, (i + shift) % size) for i in range(size)]
        pieces.append(lax.ppermute(value, axis, pairs))
    return jnp.stack(pieces)


def on_device(p_blocks, p_slots, out_slots):
    n_row = lax.axis_size("row")
    n_col = lax.axis_size("col")
    block_edge = BLK
    area = block_edge * block_edge
    rows_dev = COLS_DEV * n_col // n_row
    cells = rows_dev * COLS_DEV
    width = COLS_DEV * block_edge
    height = rows_dev * block_edge
    group = rows_dev // COLS_DEV
    row_idx = lax.axis_index("row")
    col_idx = lax.axis_index("col")

    own_ids = p_slots[0]
    grid = jnp.zeros((cells, area), jnp.bfloat16)
    grid = grid.at[jnp.where(own_ids < cells, own_ids, cells)].set(p_blocks[0], mode="drop")
    tile = (
        grid.reshape(rows_dev, COLS_DEV, block_edge, block_edge)
        .transpose(0, 2, 1, 3)
        .reshape(height, width)
    )

    column_panel = shifted_copies(tile, "row", n_row).reshape(n_col, width, width)
    row_pieces = shifted_copies(tile, "col", n_col)
    place = jnp.arange(n_col, dtype=jnp.int32)
    owner = ((row_idx - place // group) % n_row) * group + place % group
    row_panel = row_pieces[(col_idx - owner) % n_col]

    square = jnp.einsum(
        "pab,pbn->an", row_panel, column_panel, preferred_element_type=jnp.float32
    )
    square_panel = shifted_copies(square, "row", n_row).reshape(n_col, width, width)
    cube = jnp.einsum(
        "pab,pbn->an",
        row_panel.astype(jnp.float32),
        square_panel,
        precision=lax.Precision.HIGHEST,
        preferred_element_type=jnp.float32,
    )
    combined = 3.0 * square - 2.0 * cube
    new_grid = combined.reshape(rows_dev, block_edge, COLS_DEV, block_edge).transpose(0, 2, 1, 3)
    new_grid = new_grid.reshape(cells, area)
    out_ids = out_slots[0]
    picked = new_grid[jnp.minimum(out_ids, cells - 1)]
    picked = jnp.where((out_ids < cells)[:, None], picked, jnp.zeros_like(picked))
    return picked[None]


def solution(mesh):
    in_specs = (P("row", "col", None), P("row", "col"), P("row", "col"))
    out_specs = P("row", "col", None)
    return jax.shard_map(
        on_device, mesh=mesh, in_specs=in_specs, out_specs=out_specs, check_vma=False
    )
```

```python
import jax
import jax.numpy as jnp
from jax import lax
from jax.sharding import PartitionSpec as P

BLK = 64
COLS_DEV = 3


def shifted_copies(value, axis, size):
    pieces = [value]
    for shift in range(1, size):
        pairs = [(i, (i + shift) % size) for i in range(size)]
        pieces.append(lax.ppermute(value, axis, pairs))
    return jnp.stack(pieces)


def paired_copies(value, axis, size):
    pieces = [value]
    for step in range(1, size // 2):
        pairs = [(i, i ^ (2 * step)) for i in range(size)]
        pieces.append(lax.ppermute(value, axis, pairs))
    first = jnp.stack(pieces)
    second = lax.ppermute(first, axis, [(i, i ^ 1) for i in range(size)])
    both = jnp.stack([first, second], axis=1)
    return both.reshape((size,) + value.shape)


def on_device(p_blocks, p_slots, out_slots):
    n_row = lax.axis_size("row")
    n_col = lax.axis_size("col")
    block_edge = BLK
    area = block_edge * block_edge
    rows_dev = COLS_DEV * n_col // n_row
    cells = rows_dev * COLS_DEV
    width = COLS_DEV * block_edge
    height = rows_dev * block_edge
    group = rows_dev // COLS_DEV
    row_idx = lax.axis_index("row")
    col_idx = lax.axis_index("col")
    assert n_col % 2 == 0 and (n_col // 2) & (n_col // 2 - 1) == 0

    own_ids = p_slots[0]
    grid = jnp.zeros((cells, area), jnp.bfloat16)
    grid = grid.at[jnp.where(own_ids < cells, own_ids, cells)].set(p_blocks[0], mode="drop")
    tile = (
        grid.reshape(rows_dev, COLS_DEV, block_edge, block_edge)
        .transpose(0, 2, 1, 3)
        .reshape(height, width)
    )

    row_panel = paired_copies(tile, "col", n_col)
    down = shifted_copies(tile, "row", n_row).reshape(n_row * group, width, width)
    source = col_idx ^ jnp.arange(n_col, dtype=jnp.int32)
    column_panel = down[((row_idx - source // group) % n_row) * group + source % group]

    square = jnp.einsum(
        "pab,pbn->an", row_panel, column_panel, preferred_element_type=jnp.float32
    )
    square_panel = paired_copies(square, "col", n_col)
    cube = jnp.einsum(
        "pab,pbn->an",
        square_panel,
        column_panel.astype(jnp.float32),
        precision=lax.Precision.HIGHEST,
        preferred_element_type=jnp.float32,
    )
    combined = 3.0 * square - 2.0 * cube
    new_grid = combined.reshape(rows_dev, block_edge, COLS_DEV, block_edge).transpose(0, 2, 1, 3)
    new_grid = new_grid.reshape(cells, area)
    out_ids = out_slots[0]
    picked = new_grid[jnp.minimum(out_ids, cells - 1)]
    picked = jnp.where((out_ids < cells)[:, None], picked, jnp.zeros_like(picked))
    return picked[None]


def solution(mesh):
    in_specs = (P("row", "col", None), P("row", "col"), P("row", "col"))
    out_specs = P("row", "col", None)
    return jax.shard_map(
        on_device, mesh=mesh, in_specs=in_specs, out_specs=out_specs, check_vma=False
    )
```

```python
import jax
import jax.numpy as jnp
from jax import lax
from jax.sharding import PartitionSpec as P

BLK = 64
COLS_DEV = 3


def shifted_copies(value, axis, size):
    pieces = [value]
    for shift in range(1, size):
        pairs = [(i, (i + shift) % size) for i in range(size)]
        pieces.append(lax.ppermute(value, axis, pairs))
    return jnp.stack(pieces)


def paired_copies(value, axis, size):
    pieces = [value]
    for step in range(1, size // 2):
        pairs = [(i, i ^ (2 * step)) for i in range(size)]
        pieces.append(lax.ppermute(value, axis, pairs))
    second = [lax.ppermute(piece, axis, [(i, i ^ 1) for i in range(size)]) for piece in pieces]
    both = jnp.stack([jnp.stack(pieces), jnp.stack(second)], axis=1)
    return both.reshape((size,) + value.shape)


def on_device(p_blocks, p_slots, out_slots):
    n_row = lax.axis_size("row")
    n_col = lax.axis_size("col")
    block_edge = BLK
    area = block_edge * block_edge
    rows_dev = COLS_DEV * n_col // n_row
    cells = rows_dev * COLS_DEV
    width = COLS_DEV * block_edge
    height = rows_dev * block_edge
    group = rows_dev // COLS_DEV
    row_idx = lax.axis_index("row")
    col_idx = lax.axis_index("col")
    assert n_col % 2 == 0 and (n_col // 2) & (n_col // 2 - 1) == 0

    own_ids = p_slots[0]
    grid = jnp.zeros((cells, area), jnp.bfloat16)
    grid = grid.at[jnp.where(own_ids < cells, own_ids, cells)].set(p_blocks[0], mode="drop")
    tile = (
        grid.reshape(rows_dev, COLS_DEV, block_edge, block_edge)
        .transpose(0, 2, 1, 3)
        .reshape(height, width)
    )

    row_panel = paired_copies(tile, "col", n_col)
    down = shifted_copies(tile, "row", n_row).reshape(n_row * group, width, width)
    source = col_idx ^ jnp.arange(n_col, dtype=jnp.int32)
    column_panel = down[((row_idx - source // group) % n_row) * group + source % group]

    square = jnp.einsum(
        "pab,pbn->an", row_panel, column_panel, preferred_element_type=jnp.float32
    )
    square_panel = paired_copies(square, "col", n_col)
    cube = jnp.einsum(
        "pab,pbn->an",
        square_panel,
        column_panel.astype(jnp.float32),
        precision=lax.Precision.HIGHEST,
        preferred_element_type=jnp.float32,
    )
    combined = 3.0 * square - 2.0 * cube
    new_grid = combined.reshape(rows_dev, block_edge, COLS_DEV, block_edge).transpose(0, 2, 1, 3)
    new_grid = new_grid.reshape(cells, area)
    out_ids = out_slots[0]
    picked = new_grid[jnp.minimum(out_ids, cells - 1)]
    picked = jnp.where((out_ids < cells)[:, None], picked, jnp.zeros_like(picked))
    return picked[None]


def solution(mesh):
    in_specs = (P("row", "col", None), P("row", "col"), P("row", "col"))
    out_specs = P("row", "col", None)
    return jax.shard_map(
        on_device, mesh=mesh, in_specs=in_specs, out_specs=out_specs, check_vma=False
    )
```

```python
import jax
import jax.numpy as jnp
from jax import lax
from jax.sharding import PartitionSpec as P

BLK = 64
COLS_DEV = 3


def shifted_copies(value, axis, size):
    pieces = [value]
    for shift in range(1, size):
        pairs = [(i, (i + shift) % size) for i in range(size)]
        pieces.append(lax.ppermute(value, axis, pairs))
    return jnp.stack(pieces)


def paired_copies(value, axis, size):
    pieces = [value]
    for step in range(1, size // 2):
        pairs = [(i, i ^ (2 * step)) for i in range(size)]
        pieces.append(lax.ppermute(value, axis, pairs))
    second = [lax.ppermute(piece, axis, [(i, i ^ 1) for i in range(size)]) for piece in pieces]
    both = jnp.stack([jnp.stack(pieces), jnp.stack(second)], axis=1)
    return both.reshape((size,) + value.shape)


def on_device(p_blocks, p_slots, out_slots):
    n_row = lax.axis_size("row")
    n_col = lax.axis_size("col")
    block_edge = BLK
    area = block_edge * block_edge
    rows_dev = COLS_DEV * n_col // n_row
    cells = rows_dev * COLS_DEV
    width = COLS_DEV * block_edge
    height = rows_dev * block_edge
    group = rows_dev // COLS_DEV
    row_idx = lax.axis_index("row")
    col_idx = lax.axis_index("col")
    assert n_col % 2 == 0 and (n_col // 2) & (n_col // 2 - 1) == 0

    own_ids = p_slots[0]
    grid = jnp.zeros((cells, area), jnp.bfloat16)
    grid = grid.at[jnp.where(own_ids < cells, own_ids, cells)].set(p_blocks[0], mode="drop")
    tile = (
        grid.reshape(rows_dev, COLS_DEV, block_edge, block_edge)
        .transpose(0, 2, 1, 3)
        .reshape(height, width)
    )

    row_panel = paired_copies(tile, "col", n_col)
    down = shifted_copies(tile, "row", n_row).reshape(n_row * group, width, width)
    source = col_idx ^ jnp.arange(n_col, dtype=jnp.int32)
    column_panel = down[((row_idx - source // group) % n_row) * group + source % group]

    square = jnp.einsum(
        "pab,pbn->an", row_panel, column_panel, preferred_element_type=jnp.float32
    )
    square_panel = paired_copies(square, "col", n_col)
    cube = jnp.einsum(
        "pab,pbn->an",
        square_panel,
        column_panel.astype(jnp.float32),
        precision=lax.Precision.HIGHEST,
        preferred_element_type=jnp.float32,
    )
    combined = 3.0 * square - 2.0 * cube
    new_grid = combined.reshape(rows_dev, block_edge, COLS_DEV, block_edge).transpose(0, 2, 1, 3)
    new_grid = new_grid.reshape(cells, area)
    out_ids = out_slots[0]
    choose = (out_ids[:, None] == jnp.arange(cells, dtype=jnp.int32)[None, :]).astype(jnp.float32)
    picked = jnp.dot(
        choose, new_grid, precision=lax.Precision.HIGHEST, preferred_element_type=jnp.float32
    )
    return picked[None]


def solution(mesh):
    in_specs = (P("row", "col", None), P("row", "col"), P("row", "col"))
    out_specs = P("row", "col", None)
    return jax.shard_map(
        on_device, mesh=mesh, in_specs=in_specs, out_specs=out_specs, check_vma=False
    )
```

```python
import jax
import jax.numpy as jnp
from jax import lax
from jax.sharding import PartitionSpec as P

BLK = 64
COLS_DEV = 3


def shifted_copies(value, axis, size):
    pieces = [value]
    for shift in range(1, size):
        pairs = [(i, (i + shift) % size) for i in range(size)]
        pieces.append(lax.ppermute(value, axis, pairs))
    return jnp.stack(pieces)


def paired_copies(value, axis, size):
    pieces = [value]
    for step in range(1, size // 2):
        pairs = [(i, i ^ (2 * step)) for i in range(size)]
        pieces.append(lax.ppermute(value, axis, pairs))
    second = [lax.ppermute(piece, axis, [(i, i ^ 1) for i in range(size)]) for piece in pieces]
    both = jnp.stack([jnp.stack(pieces), jnp.stack(second)], axis=1)
    return both.reshape((size,) + value.shape)


def on_device(p_blocks, p_slots, out_slots):
    n_row = lax.axis_size("row")
    n_col = lax.axis_size("col")
    block_edge = BLK
    area = block_edge * block_edge
    rows_dev = COLS_DEV * n_col // n_row
    cells = rows_dev * COLS_DEV
    width = COLS_DEV * block_edge
    height = rows_dev * block_edge
    group = rows_dev // COLS_DEV
    row_idx = lax.axis_index("row")
    col_idx = lax.axis_index("col")
    assert n_col % 2 == 0 and (n_col // 2) & (n_col // 2 - 1) == 0

    own_ids = p_slots[0]
    grid = jnp.zeros((cells, area), jnp.bfloat16)
    grid = grid.at[jnp.where(own_ids < cells, own_ids, cells)].set(p_blocks[0], mode="drop")
    tile = (
        grid.reshape(rows_dev, COLS_DEV, block_edge, block_edge)
        .transpose(0, 2, 1, 3)
        .reshape(height, width)
    )

    row_panel = paired_copies(tile, "col", n_col)
    down = [tile]
    for shift in range(1, n_row):
        pairs = [(i, (i - shift) % n_row) for i in range(n_row)]
        down.append(lax.ppermute(tile, "row", pairs))
    down = jnp.stack(down).reshape(n_row * group, width, width)
    source = col_idx ^ jnp.arange(n_col, dtype=jnp.int32)
    column_panel = down[((source // group - row_idx) % n_row) * group + source % group]

    square = jnp.einsum(
        "pab,pbn->an", row_panel, column_panel, preferred_element_type=jnp.float32
    )
    square_panel = paired_copies(square, "col", n_col)
    cube = jnp.einsum(
        "pab,pbn->an",
        square_panel,
        column_panel.astype(jnp.float32),
        precision=lax.Precision.HIGHEST,
        preferred_element_type=jnp.float32,
    )
    combined = 3.0 * square - 2.0 * cube
    new_grid = combined.reshape(rows_dev, block_edge, COLS_DEV, block_edge).transpose(0, 2, 1, 3)
    new_grid = new_grid.reshape(cells, area)
    out_ids = out_slots[0]
    choose = (out_ids[:, None] == jnp.arange(cells, dtype=jnp.int32)[None, :]).astype(jnp.float32)
    picked = jnp.dot(
        choose, new_grid, precision=lax.Precision.HIGHEST, preferred_element_type=jnp.float32
    )
    return picked[None]


def solution(mesh):
    in_specs = (P("row", "col", None), P("row", "col"), P("row", "col"))
    out_specs = P("row", "col", None)
    return jax.shard_map(
        on_device, mesh=mesh, in_specs=in_specs, out_specs=out_specs, check_vma=False
    )
```
